256 devices in a mesh: gx: 32 (over x, z), gy: 8 (over y, core).
Axes of the slice: x: 4, y: 4, z: 8, core: 2. Of those that a mesh axis runs over, the one named last changes fastest.
Arguments:
- field: bfloat16 [3, 1, 48, 256, 1024], P(None, None, None, 'gx', 'gy'), may hold values from -6 to 6
- weight_x: bfloat16 [15, 48, 48], replicated, may hold values from -0.21875 to 0.21875
- weight_y: bfloat16 [15, 48, 48], replicated, may hold values from -0.21875 to 0.21875
- cotangent: bfloat16 [3, 1, 48, 256, 1024], P(None, None, None, 'gx', 'gy'), may hold values from -6 to 6
Outputs:
- output: bfloat16 [3, 1, 48, 256, 1024], P(None, None, None, 'gx', 'gy')
- field_grad: bfloat16 [3, 1, 48, 256, 1024], P(None, None, None, 'gx', 'gy')
- wx_grad: float32 [15, 48, 48], replicated
- wy_grad: float32 [15, 48, 48], replicated
The draws below stay inside these ranges and needn't reach their ends.
All inputs are finite; a program needn't handle non-finite values.
Results may differ from the reference program's by a relative error of at most 0.0054.
Values may be sent and summed in bfloat16 or wider, within the bound.
No kernel may reach another device: no remote copies, remote signals or barrier semaphores. Data moves between devices by JAX's collectives and lax.ppermute only.
A program may use at most 64 MiB of HBM per device.

```python
import jax
import jax.numpy as jnp
from jax import lax

C = 48
TAPS = 15
VARIANTS = 3
ZP = 1
NX = 256
NY = 1024


def shard_levels(key, shape, split, smallest, top_value):
    loudness = 1.0
    for dim, shards_of in split:
        heights = jax.random.uniform(jax.random.fold_in(jax.random.fold_in(key, 6), dim), (shards_of,), jnp.float32, smallest / len(split), top_value / len(split))
        loudness = loudness * jnp.repeat(jnp.exp(heights), shape[dim] // shards_of).reshape((-1,) + (1,) * (len(shape) - 1 - dim))
    return loudness


def gaussian(stream_key, extent, spread, bound, cuts=(), held_as=jnp.bfloat16):
    array = spread * jax.random.normal(stream_key, extent, jnp.float32)
    if cuts:
        array = array * shard_levels(stream_key, extent, cuts, -0.22, 0.18)
    return jnp.clip(array, -bound, bound).astype(held_as)


def setup_inputs(seed: int = 0) -> dict:
    streams_of = jax.random.split(jax.random.key(seed), 5)
    field = gaussian(streams_of[0], (VARIANTS, ZP, C, NX, NY), 1.0, 6.0, ((3, 32), (4, 8)))
    weight_x = gaussian(streams_of[1], (TAPS, C, C), (TAPS * C) ** -0.5, 0.21875)
    weight_y = gaussian(streams_of[2], (TAPS, C, C), (TAPS * C) ** -0.5, 0.21875)
    cotangent = gaussian(streams_of[3], (VARIANTS, ZP, C, NX, NY), 1.0, 6.0, ((3, 32), (4, 8)))
    return dict(field=field, weight_x=weight_x, weight_y=weight_y, cotangent=cotangent)


def pad_along(values, half, dim):
    widths = [(0, 0)] * values.ndim
    widths[dim] = (half, half)
    return jnp.pad(values, widths)

def conv_along(values, weight, dim):
    taps = weight.shape[0]
    half = (taps - 1) // 2
    padded = pad_along(values, half, dim)
    length = values.shape[dim]
    total = jnp.zeros(values.shape, jnp.float32)
    for tap in range(taps):
        piece = lax.slice_in_dim(padded, tap, tap + length, axis=dim).astype(jnp.float32)
        total = total + jnp.einsum('bzcxy,co->bzoxy', piece, weight[tap].astype(jnp.float32))
    return total

def flipped(weight):
    return jnp.transpose(jnp.flip(weight, 0), (0, 2, 1))

def tap_products(values, grads, taps, dim):
    half = (taps - 1) // 2
    padded = pad_along(values, half, dim)
    length = values.shape[dim]
    grads_wide = grads.astype(jnp.float32)
    terms = []
    for tap in range(taps):
        piece = lax.slice_in_dim(padded, tap, tap + length, axis=dim).astype(jnp.float32)
        terms.append(jnp.einsum('bzcxy,bzoxy->co', piece, grads_wide))
    return jnp.stack(terms)

def reference(field, weight_x, weight_y, cotangent):
    pre = lax.optimization_barrier(conv_along(field, weight_x, 3).astype(jnp.bfloat16))
    pre_wide = pre.astype(jnp.float32)
    act = jax.nn.gelu(pre_wide).astype(jnp.bfloat16)
    output = (field.astype(jnp.float32) + conv_along(act, weight_y, 4)).astype(jnp.bfloat16)
    act_grad = conv_along(cotangent, flipped(weight_y), 4)
    _, pull = jax.vjp(jax.nn.gelu, pre_wide)
    pre_grad = pull(act_grad)[0].astype(jnp.bfloat16)
    field_grad = (cotangent.astype(jnp.float32) + conv_along(pre_grad, flipped(weight_x), 3)).astype(jnp.bfloat16)
    count = field.shape[0] * field.shape[1] * field.shape[3] * field.shape[4]
    factor = 1.0 / jnp.sqrt(jnp.float32(count))
    taps = weight_x.shape[0]
    wy_grad = tap_products(act, cotangent, taps, 4) * factor
    wx_grad = tap_products(field, pre_grad, taps, 3) * factor
    return (output, field_grad, wx_grad, wy_grad)
```

```python
import jax
import jax.numpy as jnp
from jax import lax
from jax.sharding import PartitionSpec as P


def with_halo(cells, sides, width):
    for axis, dim in sides:
        count = lax.axis_size(axis)
        ends = count - 1
        head = lax.slice_in_dim(cells, 0, width, axis=dim)
        tail = lax.slice_in_dim(cells, cells.shape[dim] - width, cells.shape[dim], axis=dim)
        cells = jnp.concatenate(
            [
                lax.ppermute(tail, axis, [(i, (i + 1) % count) for i in range(ends)]),
                cells,
                lax.ppermute(head, axis, [((i + 1) % count, i) for i in range(ends)]),
            ],
            axis=dim,
        )
    return cells


def conv_padded(padded, weight, dim):
    taps = weight.shape[0]
    length = padded.shape[dim] - taps + 1
    total = None
    for tap in range(taps):
        piece = lax.slice_in_dim(padded, tap, tap + length, axis=dim)
        term = jnp.einsum("bzcxy,co->bzoxy", piece, weight[tap], preferred_element_type=jnp.float32)
        total = term if total is None else total + term
    return total


def flipped(weight):
    return jnp.transpose(jnp.flip(weight, 0), (0, 2, 1))


def tap_products(padded, grads, taps, dim):
    length = grads.shape[dim]
    terms = []
    for tap in range(taps):
        piece = lax.slice_in_dim(padded, tap, tap + length, axis=dim)
        terms.append(
            jnp.einsum("bzcxy,bzoxy->co", piece, grads, preferred_element_type=jnp.float32)
        )
    return jnp.stack(terms)


def activate(pre):
    return jax.nn.gelu(pre.astype(jnp.float32)).astype(jnp.bfloat16)


def global_sum(parts, axes):
    devices = 1
    for axis in axes:
        devices *= lax.axis_size(axis)
    flat = jnp.concatenate([p.reshape(-1) for p in parts])
    size = flat.shape[0]
    chunk = -(-size // devices)
    flat = jnp.pad(flat, (0, chunk * devices - size)).reshape(devices, chunk)
    mine = jnp.sum(lax.all_to_all(flat, axes, 0, 0, tiled=True), axis=0)
    full = lax.all_to_all(jnp.broadcast_to(mine[None], (devices, chunk)), axes, 0, 0, tiled=True)
    full = full.reshape(-1)
    out = []
    start = 0
    for p in parts:
        out.append(full[start:start + p.size].reshape(p.shape))
        start += p.size
    return out


def per_device(field, weight_x, weight_y, cotangent):
    taps = weight_x.shape[0]
    half = (taps - 1) // 2
    field_pad = with_halo(field, (("gx", 3),), half)
    grad_pad = with_halo(cotangent, (("gy", 4),), half)
    pre = lax.optimization_barrier(conv_padded(field_pad, weight_x, 3).astype(jnp.bfloat16))
    act = activate(pre)
    act_pad = with_halo(act, (("gy", 4),), half)
    output = (field.astype(jnp.float32) + conv_padded(act_pad, weight_y, 4)).astype(jnp.bfloat16)
    act_grad = conv_padded(grad_pad, flipped(weight_y), 4)
    _, pull = jax.vjp(jax.nn.gelu, pre.astype(jnp.float32))
    pre_grad = pull(act_grad)[0].astype(jnp.bfloat16)
    wy_term = tap_products(act_pad, cotangent, taps, 4)
    grad_xpad = with_halo(pre_grad, (("gx", 3),), half)
    field_grad = (
        cotangent.astype(jnp.float32) + conv_padded(grad_xpad, flipped(weight_x), 3)
    ).astype(jnp.bfloat16)
    wx_term = tap_products(field_pad, pre_grad, taps, 3)
    wx_sum, wy_sum = global_sum((wx_term, wy_term), ("gx", "gy"))
    count = (
        field.shape[0]
        * field.shape[1]
        * field.shape[3]
        * field.shape[4]
        * lax.axis_size("gx")
        * lax.axis_size("gy")
    )
    factor = 1.0 / jnp.sqrt(jnp.float32(count))
    return (output, field_grad, wx_sum * factor, wy_sum * factor)


def solution(mesh):
    in_specs = (P(None, None, None, "gx", "gy"), P(), P(), P(None, None, None, "gx", "gy"))
    out_specs = (P(None, None, None, "gx", "gy"), P(None, None, None, "gx", "gy"), P(), P())
    return jax.shard_map(
        per_device, mesh=mesh, in_specs=in_specs, out_specs=out_specs, check_vma=False
    )
```

```python
import jax
import jax.numpy as jnp
from jax import lax
from jax.sharding import PartitionSpec as P


def with_halo(cells, sides, width):
    for axis, dim in sides:
        count = lax.axis_size(axis)
        ends = count - 1
        head = lax.slice_in_dim(cells, 0, width, axis=dim)
        tail = lax.slice_in_dim(cells, cells.shape[dim] - width, cells.shape[dim], axis=dim)
        cells = jnp.concatenate(
            [
                lax.ppermute(tail, axis, [(i, (i + 1) % count) for i in range(ends)]),
                cells,
                lax.ppermute(head, axis, [((i + 1) % count, i) for i in range(ends)]),
            ],
            axis=dim,
        )
    return cells


def conv_padded(padded, weight, dim):
    b, z, c, x, y = padded.shape
    cells = padded.reshape(b * z, c, x, y)
    if dim == 4:
        taps = weight.reshape((1,) + weight.shape)
    else:
        taps = weight.reshape((weight.shape[0], 1) + weight.shape[1:])
    out = lax.conv_general_dilated(
        cells,
        taps,
        (1, 1),
        "VALID",
        dimension_numbers=lax.ConvDimensionNumbers((0, 1, 2, 3), (3, 2, 0, 1), (0, 1, 2, 3)),
        preferred_element_type=jnp.float32,
    )
    return out.reshape(b, z, out.shape[1], out.shape[2], out.shape[3])


def flipped(weight):
    return jnp.transpose(jnp.flip(weight, 0), (0, 2, 1))


def tap_products(padded, grads, taps, dim):
    length = grads.shape[dim]
    terms = []
    for tap in range(taps):
        piece = lax.slice_in_dim(padded, tap, tap + length, axis=dim)
        terms.append(
            jnp.einsum("bzcxy,bzoxy->co", piece, grads, preferred_element_type=jnp.float32)
        )
    return jnp.stack(terms)


def activate(pre):
    return jax.nn.gelu(pre.astype(jnp.float32)).astype(jnp.bfloat16)


def global_sum(parts, axes):
    devices = 1
    for axis in axes:
        devices *= lax.axis_size(axis)
    flat = jnp.concatenate([p.reshape(-1) for p in parts])
    size = flat.shape[0]
    chunk = -(-size // devices)
    flat = jnp.pad(flat, (0, chunk * devices - size)).reshape(devices, chunk)
    mine = jnp.sum(lax.all_to_all(flat, axes, 0, 0, tiled=True), axis=0)
    full = lax.all_to_all(jnp.broadcast_to(mine[None], (devices, chunk)), axes, 0, 0, tiled=True)
    full = full.reshape(-1)
    out = []
    start = 0
    for p in parts:
        out.append(full[start:start + p.size].reshape(p.shape))
        start += p.size
    return out


def per_device(field, weight_x, weight_y, cotangent):
    taps = weight_x.shape[0]
    half = (taps - 1) // 2
    field_pad = with_halo(field, (("gx", 3),), half)
    grad_pad = with_halo(cotangent, (("gy", 4),), half)
    pre = lax.optimization_barrier(conv_padded(field_pad, weight_x, 3).astype(jnp.bfloat16))
    act = activate(pre)
    act_pad = with_halo(act, (("gy", 4),), half)
    output = (field.astype(jnp.float32) + conv_padded(act_pad, weight_y, 4)).astype(jnp.bfloat16)
    act_grad = conv_padded(grad_pad, flipped(weight_y), 4)
    _, pull = jax.vjp(jax.nn.gelu, pre.astype(jnp.float32))
    pre_grad = pull(act_grad)[0].astype(jnp.bfloat16)
    wy_term = tap_products(act_pad, cotangent, taps, 4)
    grad_xpad = with_halo(pre_grad, (("gx", 3),), half)
    field_grad = (
        cotangent.astype(jnp.float32) + conv_padded(grad_xpad, flipped(weight_x), 3)
    ).astype(jnp.bfloat16)
    wx_term = tap_products(field_pad, pre_grad, taps, 3)
    wx_sum, wy_sum = global_sum((wx_term, wy_term), ("gx", "gy"))
    count = (
        field.shape[0]
        * field.shape[1]
        * field.shape[3]
        * field.shape[4]
        * lax.axis_size("gx")
        * lax.axis_size("gy")
    )
    factor = 1.0 / jnp.sqrt(jnp.float32(count))
    return (output, field_grad, wx_sum * factor, wy_sum * factor)


def solution(mesh):
    in_specs = (P(None, None, None, "gx", "gy"), P(), P(), P(None, None, None, "gx", "gy"))
    out_specs = (P(None, None, None, "gx", "gy"), P(None, None, None, "gx", "gy"), P(), P())
    return jax.shard_map(
        per_device, mesh=mesh, in_specs=in_specs, out_specs=out_specs, check_vma=False
    )
```

```python
import jax
import jax.numpy as jnp
from jax import lax
from jax.sharding import PartitionSpec as P


def with_halo(cells, sides, width):
    for axis, dim in sides:
        count = lax.axis_size(axis)
        ends = count - 1
        head = lax.slice_in_dim(cells, 0, width, axis=dim)
        tail = lax.slice_in_dim(cells, cells.shape[dim] - width, cells.shape[dim], axis=dim)
        cells = jnp.concatenate(
            [
                lax.ppermute(tail, axis, [(i, (i + 1) % count) for i in range(ends)]),
                cells,
                lax.ppermute(head, axis, [((i + 1) % count, i) for i in range(ends)]),
            ],
            axis=dim,
        )
    return cells


def conv_padded(padded, weight, dim):
    b, z, c, x, y = padded.shape
    cells = padded.reshape(b * z, c, x, y)
    if dim == 4:
        taps = weight.reshape((1,) + weight.shape)
    else:
        taps = weight.reshape((weight.shape[0], 1) + weight.shape[1:])
    out = lax.conv_general_dilated(
        cells,
        taps,
        (1, 1),
        "VALID",
        dimension_numbers=lax.ConvDimensionNumbers((0, 1, 2, 3), (3, 2, 0, 1), (0, 1, 2, 3)),
        preferred_element_type=jnp.float32,
    )
    return out.reshape(b, z, out.shape[1], out.shape[2], out.shape[3])


def flipped(weight):
    return jnp.transpose(jnp.flip(weight, 0), (0, 2, 1))


def tap_products(padded, grads, taps, dim):
    length = grads.shape[dim]
    terms = []
    for tap in range(taps):
        piece = lax.slice_in_dim(padded, tap, tap + length, axis=dim)
        terms.append(
            jnp.einsum("bzcxy,bzoxy->co", piece, grads, preferred_element_type=jnp.float32)
        )
    return jnp.stack(terms)


def activate(pre):
    return jax.nn.gelu(pre.astype(jnp.float32)).astype(jnp.bfloat16)


def tree_sum(values, axis):
    count = lax.axis_size(axis)
    step = 1
    while step < count:
        values = values + lax.ppermute(values, axis, [(i, i ^ step) for i in range(count)])
        step *= 2
    return values


def global_sum(parts, scatter_axis, tree_axis, factor):
    devices = lax.axis_size(scatter_axis)
    lanes = 128
    flat = jnp.concatenate([p.reshape(-1) for p in parts])
    size = flat.shape[0]
    rows = -(-size // (devices * lanes))
    flat = jnp.pad(flat, (0, rows * devices * lanes - size)).reshape(devices, rows, lanes)
    mine = jnp.sum(lax.all_to_all(flat, scatter_axis, 0, 0, tiled=True), axis=0)
    mine = tree_sum(mine, tree_axis) * factor
    full = lax.all_to_all(
        jnp.broadcast_to(mine[None], (devices, rows, lanes)), scatter_axis, 0, 0, tiled=True
    )
    full = full.reshape(-1)
    out = []
    start = 0
    for p in parts:
        out.append(full[start:start + p.size].reshape(p.shape))
        start += p.size
    return out


def per_device(field, weight_x, weight_y, cotangent):
    taps = weight_x.shape[0]
    half = (taps - 1) // 2
    field_pad = with_halo(field, (("gx", 3),), half)
    pre = lax.optimization_barrier(conv_padded(field_pad, weight_x, 3).astype(jnp.bfloat16))
    act = activate(pre)
    paired = with_halo(jnp.stack((act, cotangent)), (("gy", 5),), half)
    act_pad = paired[0]
    grad_pad = paired[1]
    output = (field.astype(jnp.float32) + conv_padded(act_pad, weight_y, 4)).astype(jnp.bfloat16)
    act_grad = conv_padded(grad_pad, flipped(weight_y), 4)
    _, pull = jax.vjp(jax.nn.gelu, pre.astype(jnp.float32))
    pre_grad = pull(act_grad)[0].astype(jnp.bfloat16)
    wy_term = tap_products(act_pad, cotangent, taps, 4)
    grad_xpad = with_halo(pre_grad, (("gx", 3),), half)
    field_grad = (
        cotangent.astype(jnp.float32) + conv_padded(grad_xpad, flipped(weight_x), 3)
    ).astype(jnp.bfloat16)
    wx_term = tap_products(field_pad, pre_grad, taps, 3)
    count = (
        field.shape[0]
        * field.shape[1]
        * field.shape[3]
        * field.shape[4]
        * lax.axis_size("gx")
        * lax.axis_size("gy")
    )
    factor = 1.0 / jnp.sqrt(jnp.float32(count))
    wx_sum, wy_sum = global_sum((wx_term, wy_term), "gx", "gy", factor)
    return (output, field_grad, wx_sum, wy_sum)


def solution(mesh):
    in_specs = (P(None, None, None, "gx", "gy"), P(), P(), P(None, None, None, "gx", "gy"))
    out_specs = (P(None, None, None, "gx", "gy"), P(None, None, None, "gx", "gy"), P(), P())
    return jax.shard_map(
        per_device, mesh=mesh, in_specs=in_specs, out_specs=out_specs, check_vma=False
    )
```

```python
import jax
import jax.numpy as jnp
from jax import lax
from jax.sharding import PartitionSpec as P


def with_halo(cells, sides, width):
    for axis, dim in sides:
        count = lax.axis_size(axis)
        ends = count - 1
        head = lax.slice_in_dim(cells, 0, width, axis=dim)
        tail = lax.slice_in_dim(cells, cells.shape[dim] - width, cells.shape[dim], axis=dim)
        cells = jnp.concatenate(
            [
                lax.ppermute(tail, axis, [(i, (i + 1) % count) for i in range(ends)]),
                cells,
                lax.ppermute(head, axis, [((i + 1) % count, i) for i in range(ends)]),
            ],
            axis=dim,
        )
    return cells


def conv_padded(padded, weight, dim):
    taps = weight.shape[0]
    length = padded.shape[dim] - taps + 1
    windows = jnp.stack(
        [lax.slice_in_dim(padded, tap, tap + length, axis=dim) for tap in range(taps)]
    )
    return jnp.einsum("kbzcxy,kco->bzoxy", windows, weight, preferred_element_type=jnp.float32)

def flipped(weight):
    return jnp.transpose(jnp.flip(weight, 0), (0, 2, 1))


def tap_products(padded, grads, taps, dim):
    length = grads.shape[dim]
    windows = jnp.stack(
        [lax.slice_in_dim(padded, tap, tap + length, axis=dim) for tap in range(taps)]
    )
    return jnp.einsum("kbzcxy,bzoxy->kco", windows, grads, preferred_element_type=jnp.float32)

def activate(pre):
    return jax.nn.gelu(pre.astype(jnp.float32)).astype(jnp.bfloat16)


def tree_sum(values, axis):
    count = lax.axis_size(axis)
    step = 1
    while step < count:
        values = values + lax.ppermute(values, axis, [(i, i ^ step) for i in range(count)])
        step *= 2
    return values


def global_sum(parts, scatter_axis, tree_axis, factor):
    devices = lax.axis_size(scatter_axis)
    lanes = 128
    flat = jnp.concatenate([p.reshape(-1) for p in parts])
    size = flat.shape[0]
    rows = -(-size // (devices * lanes))
    flat = jnp.pad(flat, (0, rows * devices * lanes - size)).reshape(devices, rows, lanes)
    mine = jnp.sum(lax.all_to_all(flat, scatter_axis, 0, 0, tiled=True), axis=0)
    mine = tree_sum(mine, tree_axis) * factor
    full = lax.all_to_all(
        jnp.broadcast_to(mine[None], (devices, rows, lanes)), scatter_axis, 0, 0, tiled=True
    )
    full = full.reshape(-1)
    out = []
    start = 0
    for p in parts:
        out.append(full[start:start + p.size].reshape(p.shape))
        start += p.size
    return out


def per_device(field, weight_x, weight_y, cotangent):
    taps = weight_x.shape[0]
    half = (taps - 1) // 2
    field_pad = with_halo(field, (("gx", 3),), half)
    pre = lax.optimization_barrier(conv_padded(field_pad, weight_x, 3).astype(jnp.bfloat16))
    act = activate(pre)
    paired = with_halo(jnp.stack((act, cotangent)), (("gy", 5),), half)
    act_pad = paired[0]
    grad_pad = paired[1]
    output = (field.astype(jnp.float32) + conv_padded(act_pad, weight_y, 4)).astype(jnp.bfloat16)
    act_grad = conv_padded(grad_pad, flipped(weight_y), 4)
    _, pull = jax.vjp(jax.nn.gelu, pre.astype(jnp.float32))
    pre_grad = pull(act_grad)[0].astype(jnp.bfloat16)
    wy_term = tap_products(act_pad, cotangent, taps, 4)
    grad_xpad = with_halo(pre_grad, (("gx", 3),), half)
    field_grad = (
        cotangent.astype(jnp.float32) + conv_padded(grad_xpad, flipped(weight_x), 3)
    ).astype(jnp.bfloat16)
    wx_term = tap_products(field_pad, pre_grad, taps, 3)
    count = (
        field.shape[0]
        * field.shape[1]
        * field.shape[3]
        * field.shape[4]
        * lax.axis_size("gx")
        * lax.axis_size("gy")
    )
    factor = 1.0 / jnp.sqrt(jnp.float32(count))
    wx_sum, wy_sum = global_sum((wx_term, wy_term), "gx", "gy", factor)
    return (output, field_grad, wx_sum, wy_sum)


def solution(mesh):
    in_specs = (P(None, None, None, "gx", "gy"), P(), P(), P(None, None, None, "gx", "gy"))
    out_specs = (P(None, None, None, "gx", "gy"), P(None, None, None, "gx", "gy"), P(), P())
    return jax.shard_map(
        per_device, mesh=mesh, in_specs=in_specs, out_specs=out_specs, check_vma=False
    )
```

```python
import jax
import jax.numpy as jnp
from jax import lax
from jax.sharding import PartitionSpec as P


def with_halo(cells, sides, width):
    for axis, dim in sides:
        count = lax.axis_size(axis)
        ends = count - 1
        head = lax.slice_in_dim(cells, 0, width, axis=dim)
        tail = lax.slice_in_dim(cells, cells.shape[dim] - width, cells.shape[dim], axis=dim)
        cells = jnp.concatenate(
            [
                lax.ppermute(tail, axis, [(i, (i + 1) % count) for i in range(ends)]),
                cells,
                lax.ppermute(head, axis, [((i + 1) % count, i) for i in range(ends)]),
            ],
            axis=dim,
        )
    return cells


def conv_unfolded(padded, weight, dim):
    taps = weight.shape[0]
    length = padded.shape[dim] - taps + 1
    windows = jnp.stack(
        [lax.slice_in_dim(padded, tap, tap + length, axis=dim) for tap in range(taps)]
    )
    return jnp.einsum("kbzcxy,kco->bzoxy", windows, weight, preferred_element_type=jnp.float32)


def conv_lax(padded, weight, dim):
    b, z, c, x, y = padded.shape
    cells = padded.reshape(b * z, c, x, y)
    if dim == 4:
        taps = weight.reshape((1,) + weight.shape)
    else:
        taps = weight.reshape((weight.shape[0], 1) + weight.shape[1:])
    out = lax.conv_general_dilated(
        cells,
        taps,
        (1, 1),
        "VALID",
        dimension_numbers=lax.ConvDimensionNumbers((0, 1, 2, 3), (3, 2, 0, 1), (0, 1, 2, 3)),
        preferred_element_type=jnp.float32,
    )
    return out.reshape(b, z, out.shape[1], out.shape[2], out.shape[3])


def conv_padded(padded, weight, dim, native=False):
    if native:
        return conv_lax(padded, weight, dim)
    return conv_unfolded(padded, weight, dim)

def flipped(weight):
    return jnp.transpose(jnp.flip(weight, 0), (0, 2, 1))


def tap_products(padded, grads, taps, dim):
    length = grads.shape[dim]
    windows = jnp.stack(
        [lax.slice_in_dim(padded, tap, tap + length, axis=dim) for tap in range(taps)]
    )
    return jnp.einsum("kbzcxy,bzoxy->kco", windows, grads, preferred_element_type=jnp.float32)

def activate(pre):
    return jax.nn.gelu(pre.astype(jnp.float32)).astype(jnp.bfloat16)


def tree_sum(values, axis):
    count = lax.axis_size(axis)
    step = 1
    while step < count:
        values = values + lax.ppermute(values, axis, [(i, i ^ step) for i in range(count)])
        step *= 2
    return values


def global_sum(parts, scatter_axis, tree_axis, factor):
    devices = lax.axis_size(scatter_axis)
    lanes = 128
    flat = jnp.concatenate([p.reshape(-1) for p in parts])
    size = flat.shape[0]
    rows = -(-size // (devices * lanes))
    flat = jnp.pad(flat, (0, rows * devices * lanes - size)).reshape(devices, rows, lanes)
    mine = jnp.sum(lax.all_to_all(flat, scatter_axis, 0, 0, tiled=True), axis=0)
    mine = tree_sum(mine, tree_axis) * factor
    full = lax.all_to_all(
        jnp.broadcast_to(mine[None], (devices, rows, lanes)), scatter_axis, 0, 0, tiled=True
    )
    full = full.reshape(-1)
    out = []
    start = 0
    for p in parts:
        out.append(full[start:start + p.size].reshape(p.shape))
        start += p.size
    return out


def per_device(field, weight_x, weight_y, cotangent):
    taps = weight_x.shape[0]
    half = (taps - 1) // 2
    field_pad = with_halo(field, (("gx", 3),), half)
    pre = lax.optimization_barrier(conv_padded(field_pad, weight_x, 3).astype(jnp.bfloat16))
    act = activate(pre)
    paired = with_halo(jnp.stack((act, cotangent)), (("gy", 5),), half)
    act_pad = paired[0]
    grad_pad = paired[1]
    output = (field.astype(jnp.float32) + conv_padded(act_pad, weight_y, 4)).astype(jnp.bfloat16)
    act_grad = conv_padded(grad_pad, flipped(weight_y), 4)
    _, pull = jax.vjp(jax.nn.gelu, pre.astype(jnp.float32))
    pre_grad = pull(act_grad)[0].astype(jnp.bfloat16)
    wy_term = tap_products(act_pad, cotangent, taps, 4)
    grad_xpad = with_halo(pre_grad, (("gx", 3),), half)
    field_grad = (
        cotangent.astype(jnp.float32) + conv_padded(grad_xpad, flipped(weight_x), 3, True)
    ).astype(jnp.bfloat16)
    wx_term = tap_products(field_pad, pre_grad, taps, 3)
    count = (
        field.shape[0]
        * field.shape[1]
        * field.shape[3]
        * field.shape[4]
        * lax.axis_size("gx")
        * lax.axis_size("gy")
    )
    factor = 1.0 / jnp.sqrt(jnp.float32(count))
    wx_sum, wy_sum = global_sum((wx_term, wy_term), "gx", "gy", factor)
    return (output, field_grad, wx_sum, wy_sum)


def solution(mesh):
    in_specs = (P(None, None, None, "gx", "gy"), P(), P(), P(None, None, None, "gx", "gy"))
    out_specs = (P(None, None, None, "gx", "gy"), P(None, None, None, "gx", "gy"), P(), P())
    return jax.shard_map(
        per_device, mesh=mesh, in_specs=in_specs, out_specs=out_specs, check_vma=False
    )
```

```python
import jax
import jax.numpy as jnp
from jax import lax
from jax.sharding import PartitionSpec as P


def with_halo(cells, sides, width):
    for axis, dim in sides:
        count = lax.axis_size(axis)
        ends = count - 1
        head = lax.slice_in_dim(cells, 0, width, axis=dim)
        tail = lax.slice_in_dim(cells, cells.shape[dim] - width, cells.shape[dim], axis=dim)
        cells = jnp.concatenate(
            [
                lax.ppermute(tail, axis, [(i, (i + 1) % count) for i in range(ends)]),
                cells,
                lax.ppermute(head, axis, [((i + 1) % count, i) for i in range(ends)]),
            ],
            axis=dim,
        )
    return cells


def conv_unfolded(padded, weight, dim):
    taps = weight.shape[0]
    length = padded.shape[dim] - taps + 1
    windows = jnp.stack(
        [lax.slice_in_dim(padded, tap, tap + length, axis=dim) for tap in range(taps)]
    )
    return jnp.einsum("kbzcxy,kco->bzoxy", windows, weight, preferred_element_type=jnp.float32)


def conv_lax(padded, weight, dim):
    b, z, c, x, y = padded.shape
    cells = padded.reshape(b * z, c, x, y)
    if dim == 4:
        taps = weight.reshape((1,) + weight.shape)
    else:
        taps = weight.reshape((weight.shape[0], 1) + weight.shape[1:])
    out = lax.conv_general_dilated(
        cells,
        taps,
        (1, 1),
        "VALID",
        dimension_numbers=lax.ConvDimensionNumbers((0, 1, 2, 3), (3, 2, 0, 1), (0, 1, 2, 3)),
        preferred_element_type=jnp.float32,
    )
    return out.reshape(b, z, out.shape[1], out.shape[2], out.shape[3])


def conv_padded(padded, weight, dim, native=False):
    if native:
        return conv_lax(padded, weight, dim)
    return conv_unfolded(padded, weight, dim)

def flipped(weight):
    return jnp.transpose(jnp.flip(weight, 0), (0, 2, 1))


def tap_products(padded, grads, taps, dim):
    length = grads.shape[dim]
    windows = jnp.stack(
        [lax.slice_in_dim(padded, tap, tap + length, axis=dim) for tap in range(taps)]
    )
    return jnp.einsum("kbzcxy,bzoxy->kco", windows, grads, preferred_element_type=jnp.float32)

def activate(pre):
    return jax.nn.gelu(pre.astype(jnp.float32)).astype(jnp.bfloat16)


def tree_sum(values, axis):
    count = lax.axis_size(axis)
    step = 1
    while step < count:
        values = values + lax.ppermute(values, axis, [(i, i ^ step) for i in range(count)])
        step *= 2
    return values


def global_sum(parts, scatter_axis, tree_axis, factor):
    devices = lax.axis_size(scatter_axis)
    lanes = 128
    flat = jnp.concatenate([p.reshape(-1) for p in parts])
    size = flat.shape[0]
    rows = -(-size // (devices * lanes))
    flat = jnp.pad(flat, (0, rows * devices * lanes - size)).reshape(devices, rows, lanes)
    mine = jnp.sum(lax.all_to_all(flat, scatter_axis, 0, 0, tiled=True), axis=0)
    mine = tree_sum(mine, tree_axis) * factor
    full = lax.all_to_all(
        jnp.broadcast_to(mine[None], (devices, rows, lanes)), scatter_axis, 0, 0, tiled=True
    )
    full = full.reshape(-1)
    out = []
    start = 0
    for p in parts:
        out.append(full[start:start + p.size].reshape(p.shape))
        start += p.size
    return out


def per_device(field, weight_x, weight_y, cotangent):
    taps = weight_x.shape[0]
    half = (taps - 1) // 2
    field_pad = with_halo(field, (("gx", 3),), half)
    pre = lax.optimization_barrier(conv_padded(field_pad, weight_x, 3).astype(jnp.bfloat16))
    act = activate(pre)
    paired = with_halo(jnp.stack((act, cotangent)), (("gy", 5),), half)
    act_pad = paired[0]
    grad_pad = paired[1]
    output = (field.astype(jnp.float32) + conv_padded(act_pad, weight_y, 4)).astype(jnp.bfloat16)
    length = field.shape[4]
    grad_windows = jnp.stack(
        [lax.slice_in_dim(grad_pad, tap, tap + length, axis=4) for tap in range(taps)]
    )
    act_grad = jnp.einsum(
        "kbzcxy,kco->bzoxy", grad_windows, flipped(weight_y), preferred_element_type=jnp.float32
    )
    _, pull = jax.vjp(jax.nn.gelu, pre.astype(jnp.float32))
    pre_grad = pull(act_grad)[0].astype(jnp.bfloat16)
    wy_term = jnp.flip(
        jnp.einsum("kbzoxy,bzcxy->kco", grad_windows, act, preferred_element_type=jnp.float32), 0
    )
    grad_xpad = with_halo(pre_grad, (("gx", 3),), half)
    field_grad = (
        cotangent.astype(jnp.float32) + conv_padded(grad_xpad, flipped(weight_x), 3, True)
    ).astype(jnp.bfloat16)
    wx_term = tap_products(field_pad, pre_grad, taps, 3)
    count = (
        field.shape[0]
        * field.shape[1]
        * field.shape[3]
        * field.shape[4]
        * lax.axis_size("gx")
        * lax.axis_size("gy")
    )
    factor = 1.0 / jnp.sqrt(jnp.float32(count))
    wx_sum, wy_sum = global_sum((wx_term, wy_term), "gx", "gy", factor)
    return (output, field_grad, wx_sum, wy_sum)


def solution(mesh):
    in_specs = (P(None, None, None, "gx", "gy"), P(), P(), P(None, None, None, "gx", "gy"))
    out_specs = (P(None, None, None, "gx", "gy"), P(None, None, None, "gx", "gy"), P(), P())
    return jax.shard_map(
        per_device, mesh=mesh, in_specs=in_specs, out_specs=out_specs, check_vma=False
    )
```
